128 devices in a mesh: scan: 8 (over x, y_lo), det: 16 (over y_hi, z, core).
Axes of the slice: x: 4, y: 4 (y_hi: 2, y_lo: 2; y = y_hi * 2 + y_lo), z: 4, core: 2. Of those that a mesh axis runs over, the one named last changes fastest.
Arguments:
- data: float32 [2, 512, 2, 256, 256], P(None, 'scan', None, 'det'), may hold values from -6 to 6
- wigner: float32 [2, 512, 2, 256, 256], P(None, ('scan', 'det')), may hold values from -6 to 6
Outputs:
- deconvolved: float32 [2, 512, 2, 256, 256], P(None, 'scan', None, 'det')
The draws below stay inside these ranges and needn't reach their ends.
All inputs are finite; a program needn't handle non-finite values.
Results may differ from the reference program's by a relative error of at most 0.0001.
Values sent between devices are 32-bit elements; how exact they have to be, the bound alone decides.
No kernel may reach another device: no remote copies, remote signals or barrier semaphores. Data moves between devices by JAX's collectives and lax.ppermute only.
A program may use at most 128 MiB of HBM per device.

```python
import math
import jax
import jax.numpy as jnp

SR = 512
DET = 256
FREQS = 2


def shard_levels(key, shape, split, smallest, top_value):
    def one(position, blocks):
        draws = jax.random.uniform(jax.random.fold_in(jax.random.fold_in(key, 6), position), (blocks,), jnp.float32, smallest / len(split), top_value / len(split))
        return jnp.repeat(jnp.exp(draws), shape[position] // blocks).reshape((-1,) + (1,) * (len(shape) - position - 1))

    level = one(*split[0])
    for cut in split[1:]:
        level = level * one(*cut)
    return level


def scatter_about(own_key, dims, scale, limit, cuts=(), held_as=jnp.bfloat16):
    result = jax.random.normal(own_key, dims, jnp.float32) * scale
    if len(cuts) > 0:
        result = shard_levels(own_key, dims, cuts, -0.22, 0.18) * result
    return jnp.clip(result, min=-limit, max=limit).astype(held_as)


def setup_inputs(seed: int = 0) -> dict:
    key_list = jax.random.split(jax.random.key(seed), 3)
    data = scatter_about(key_list[0], (2, SR, FREQS, DET, DET), 1.0, 6.0, ((1, 8), (3, 16)), jnp.float32)
    wigner = scatter_about(key_list[1], (2, SR, FREQS, DET, DET), 1.0, 6.0, ((1, 128),), jnp.float32)
    return {"data": data, "wigner": wigner}


eps_wiener = 0.1

def reference(data, wigner):
    results = []
    for freq_index in range(FREQS):
        planes = data[0, :, freq_index] + 1j * data[1, :, freq_index]
        spectra = jnp.fft.fft(planes, axis=0) / math.sqrt(SR)
        spatial = jnp.fft.ifft2(spectra, axes=(1, 2)) * DET
        kernel = (wigner[0, :, freq_index] + 1j * wigner[1, :, freq_index]).transpose(0, 2, 1)
        power = kernel.real * kernel.real + kernel.imag * kernel.imag + eps_wiener
        filtered = spatial * jnp.conj(kernel) / power
        output_planes = jnp.fft.fft2(filtered, axes=(1, 2)) / DET
        results.append(jnp.stack([output_planes.real, output_planes.imag]).astype(jnp.float32))
    return jnp.stack(results, axis=2)
```

```python
import math

import jax
import jax.numpy as jnp
from jax import lax
from jax.sharding import PartitionSpec as P

eps_wiener = 0.1
HIGHEST = lax.Precision.HIGHEST


def angles(rows, cols, count):
    product = (rows[:, None] * cols[None, :]) % count
    return product.astype(jnp.float32) * (2.0 * math.pi / count)


def tables(count, sign):
    indices = jnp.arange(count, dtype=jnp.int32)
    phases = angles(indices, indices, count)
    norm_scale = 1.0 / math.sqrt(count)
    return (jnp.cos(phases) * norm_scale, sign * jnp.sin(phases) * norm_scale)


def row_table(rows_total, blocks):
    cosine, sines = tables(rows_total, 1.0)
    top = jnp.stack([cosine, sines], axis=1)
    bottom = jnp.stack([-sines, cosine], axis=1)
    full = jnp.stack([top, bottom], axis=1)
    local = rows_total // blocks
    full = full.reshape(rows_total, 2, 2, blocks, local)
    full = full.transpose(0, 1, 3, 2, 4)
    return full.reshape(2 * rows_total, 2 * rows_total)


def product_form(form, left, right):
    return jnp.einsum(form, left, right, precision=HIGHEST)


def pair_right(real_in, imag_in, form, cosine, sines):
    real_out = product_form(form, real_in, cosine) - product_form(form, imag_in, sines)
    imag_out = product_form(form, real_in, sines) + product_form(form, imag_in, cosine)
    return (real_out, imag_out)


def shards(data, wigner):
    n_scan = lax.axis_size("scan")
    n_det = lax.axis_size("det")
    n_all = n_scan * n_det
    _, local_rows, freq_count, local_det, detector = data.shape
    rows_total = local_rows * n_scan
    det_total = local_det * n_det
    col_chunk = detector // n_scan
    q_block = rows_total // n_all

    send = data.reshape(2, local_rows, freq_count, local_det, n_scan, col_chunk)
    send = send.transpose(4, 0, 1, 2, 3, 5)
    got = lax.all_to_all(send, "scan", 0, 0, tiled=True)
    got = got.reshape(2 * rows_total, freq_count * local_det * col_chunk)

    spectra = jnp.dot(row_table(rows_total, n_scan), got, precision=HIGHEST)
    spectra = spectra.reshape(rows_total, 2, freq_count, local_det, col_chunk)
    spectra = spectra.reshape(n_all, q_block, 2, freq_count, local_det, col_chunk)

    frames = lax.all_to_all(spectra, ("scan", "det"), 0, 0, tiled=True)
    frames = frames.reshape(n_scan, n_det, q_block, 2, freq_count, local_det, col_chunk)
    frames = frames.transpose(3, 2, 4, 1, 5, 0, 6).reshape(2, q_block, freq_count, det_total, detector)

    inv_cos, inv_sin = tables(detector, 1.0)
    fwd_cos, fwd_sin = tables(detector, -1.0)
    half_real, half_imag = pair_right(frames[0], frames[1], "qfab,by->qfay", inv_cos, inv_sin)
    field_real, field_imag = pair_right(half_real, half_imag, "qfay,xa->qfyx", inv_cos, inv_sin)
    kernel_real = wigner[0]
    kernel_imag = wigner[1]
    power = kernel_real * kernel_real + kernel_imag * kernel_imag + eps_wiener
    filtered_real = (field_real * kernel_real + field_imag * kernel_imag) / power
    filtered_imag = (field_imag * kernel_real - field_real * kernel_imag) / power
    half_real, half_imag = pair_right(filtered_real, filtered_imag, "qfyx,ax->qfya", fwd_cos, fwd_sin)
    plane_real, plane_imag = pair_right(half_real, half_imag, "qfya,by->qfab", fwd_cos, fwd_sin)
    planes = jnp.stack([plane_real, plane_imag])

    planes = planes.reshape(2, q_block, freq_count, n_det, local_det, detector)
    planes = planes.transpose(3, 0, 1, 2, 4, 5)
    back = lax.all_to_all(planes, "det", 0, 0, tiled=True)
    back = back.transpose(1, 0, 2, 3, 4, 5)
    return back.reshape(2, n_det * q_block, freq_count, local_det, detector)


def solution(mesh):
    in_specs = (P(None, "scan", None, "det", None), P(None, ("scan", "det"), None, None, None))
    out_specs = P(None, "scan", None, "det", None)
    return jax.shard_map(shards, mesh=mesh, in_specs=in_specs, out_specs=out_specs, check_vma=False)
```

```python
import math

import jax
import jax.numpy as jnp
from jax import lax
from jax.sharding import PartitionSpec as P

eps_wiener = 0.1
HIGHEST = lax.Precision.HIGHEST


def angles(rows, cols, count):
    product = (rows[:, None] * cols[None, :]) % count
    return product.astype(jnp.float32) * (2.0 * math.pi / count)


def tables(count, sign):
    indices = jnp.arange(count, dtype=jnp.int32)
    phases = angles(indices, indices, count)
    norm_scale = 1.0 / math.sqrt(count)
    return (jnp.cos(phases) * norm_scale, sign * jnp.sin(phases) * norm_scale)


def row_table(rows_total, blocks):
    cosine, sines = tables(rows_total, 1.0)
    top = jnp.stack([cosine, sines], axis=1)
    bottom = jnp.stack([-sines, cosine], axis=1)
    full = jnp.stack([top, bottom], axis=1)
    local = rows_total // blocks
    full = full.reshape(rows_total, 2, 2, blocks, local)
    full = full.transpose(0, 1, 3, 2, 4)
    return full.reshape(2 * rows_total, 2 * rows_total)


def product_form(form, left, right):
    return jnp.einsum(form, left, right, precision=HIGHEST)


def pair_right(real_in, imag_in, form, cosine, sines):
    real_out = product_form(form, real_in, cosine) - product_form(form, imag_in, sines)
    imag_out = product_form(form, real_in, sines) + product_form(form, imag_in, cosine)
    return (real_out, imag_out)


def shards(data, wigner):
    n_scan = lax.axis_size("scan")
    n_det = lax.axis_size("det")
    n_all = n_scan * n_det
    _, local_rows, freq_count, local_det, detector = data.shape
    rows_total = local_rows * n_scan
    det_total = local_det * n_det
    q_block = rows_total // n_all
    group = freq_count * local_det // n_scan
    per_freq = n_scan // freq_count
    sub = local_det // per_freq

    send = data.reshape(2, local_rows, n_scan, sub, detector).transpose(2, 0, 1, 3, 4)
    send = send.reshape(n_scan, 2 * local_rows, sub * detector)
    got = lax.all_to_all(send, "scan", 0, 0, tiled=True)
    got = got.reshape(2 * rows_total, sub * detector)

    spectra = jnp.dot(row_table(rows_total, n_scan), got, precision=HIGHEST)
    spectra = spectra.reshape(n_all, q_block * 2, sub * detector)

    frames = lax.all_to_all(spectra, ("scan", "det"), 0, 0, tiled=True)
    frames = frames.reshape(freq_count, per_freq, n_det, q_block, 2, sub, detector)
    frames = frames.transpose(3, 0, 4, 1, 2, 5, 6).reshape(q_block, freq_count, 2, det_total, detector)
    frame_real = frames[:, :, 0]
    frame_imag = frames[:, :, 1]

    pos = jnp.arange(det_total, dtype=jnp.int32)
    h_of = pos // (n_det * sub)
    d_of = (pos // sub) % n_det
    a_of = local_det * d_of + sub * h_of + pos % sub
    cols = jnp.arange(detector, dtype=jnp.int32)
    scale = 1.0 / math.sqrt(detector)
    row_phase = angles(a_of, cols, detector)
    perm_cos = jnp.cos(row_phase) * scale
    perm_sin = jnp.sin(row_phase) * scale

    inv_cos, inv_sin = tables(detector, 1.0)
    fwd_cos, fwd_sin = tables(detector, -1.0)
    half_real, half_imag = pair_right(frame_real, frame_imag, "qfab,by->qfay", inv_cos, inv_sin)
    field_real, field_imag = pair_right(half_real, half_imag, "qfay,ax->qfyx", perm_cos, perm_sin)
    kernel_real = wigner[0]
    kernel_imag = wigner[1]
    power = kernel_real * kernel_real + kernel_imag * kernel_imag + eps_wiener
    filtered_real = (field_real * kernel_real + field_imag * kernel_imag) / power
    filtered_imag = (field_imag * kernel_real - field_real * kernel_imag) / power
    half_real, half_imag = pair_right(filtered_real, filtered_imag, "qfyx,ax->qfya", fwd_cos, fwd_sin)
    plane_real, plane_imag = pair_right(half_real, half_imag, "qfya,by->qfab", fwd_cos, fwd_sin)
    planes = jnp.stack([plane_real, plane_imag])

    planes = planes.reshape(2, q_block, freq_count, n_det, local_det, detector)
    planes = planes.transpose(3, 0, 1, 2, 4, 5).reshape(n_det, 2 * q_block * freq_count * local_det, detector)
    back = lax.all_to_all(planes, "det", 0, 0, tiled=True)
    back = back.reshape(n_det, 2, q_block, freq_count, local_det, detector).transpose(1, 0, 2, 3, 4, 5)
    return back.reshape(2, n_det * q_block, freq_count, local_det, detector)


def solution(mesh):
    in_specs = (P(None, "scan", None, "det", None), P(None, ("scan", "det"), None, None, None))
    out_specs = P(None, "scan", None, "det", None)
    return jax.shard_map(shards, mesh=mesh, in_specs=in_specs, out_specs=out_specs, check_vma=False)
```

```python
import math

import jax
import jax.numpy as jnp
from jax import lax
from jax.sharding import PartitionSpec as P

eps_wiener = 0.1
MATMUL_PRECISION = lax.Precision.HIGH


def angles(rows, cols, count):
    product = (rows[:, None] * cols[None, :]) % count
    return product.astype(jnp.float32) * (2.0 * math.pi / count)


def tables(count, sign):
    indices = jnp.arange(count, dtype=jnp.int32)
    phases = angles(indices, indices, count)
    norm_scale = 1.0 / math.sqrt(count)
    return (jnp.cos(phases) * norm_scale, sign * jnp.sin(phases) * norm_scale)


def row_table(rows_total, blocks):
    cosine, sines = tables(rows_total, 1.0)
    top = jnp.stack([cosine, sines], axis=1)
    bottom = jnp.stack([-sines, cosine], axis=1)
    full = jnp.stack([top, bottom], axis=1)
    local = rows_total // blocks
    full = full.reshape(rows_total, 2, 2, blocks, local)
    full = full.transpose(0, 1, 3, 2, 4)
    return full.reshape(2 * rows_total, 2 * rows_total)


def product_form(form, left, right):
    return jnp.einsum(form, left, right, precision=MATMUL_PRECISION)


def pair_right(real_in, imag_in, form, cosine, sines):
    real_out = product_form(form, real_in, cosine) - product_form(form, imag_in, sines)
    imag_out = product_form(form, real_in, sines) + product_form(form, imag_in, cosine)
    return (real_out, imag_out)


def shards(data, wigner):
    n_scan = lax.axis_size("scan")
    n_det = lax.axis_size("det")
    n_all = n_scan * n_det
    _, local_rows, freq_count, local_det, detector = data.shape
    rows_total = local_rows * n_scan
    det_total = local_det * n_det
    q_block = rows_total // n_all
    group = freq_count * local_det // n_scan
    per_freq = n_scan // freq_count
    sub = local_det // per_freq

    send = data.reshape(2, local_rows, n_scan, sub, detector).transpose(2, 0, 1, 3, 4)
    send = send.reshape(n_scan, 2 * local_rows, sub * detector)
    got = lax.all_to_all(send, "scan", 0, 0, tiled=True)
    got = got.reshape(2 * rows_total, sub * detector)

    spectra = jnp.dot(row_table(rows_total, n_scan), got, precision=MATMUL_PRECISION)
    spectra = spectra.reshape(n_all, q_block * 2, sub * detector)

    frames = lax.all_to_all(spectra, ("scan", "det"), 0, 0, tiled=True)
    frames = frames.reshape(freq_count, per_freq, n_det, q_block, 2, sub, detector)
    frames = frames.transpose(3, 0, 4, 1, 2, 5, 6).reshape(q_block, freq_count, 2, det_total, detector)
    frame_real = frames[:, :, 0]
    frame_imag = frames[:, :, 1]

    pos = jnp.arange(det_total, dtype=jnp.int32)
    h_of = pos // (n_det * sub)
    d_of = (pos // sub) % n_det
    a_of = local_det * d_of + sub * h_of + pos % sub
    cols = jnp.arange(detector, dtype=jnp.int32)
    scale = 1.0 / math.sqrt(detector)
    row_phase = angles(a_of, cols, detector)
    perm_cos = jnp.cos(row_phase) * scale
    perm_sin = jnp.sin(row_phase) * scale

    inv_cos, inv_sin = tables(detector, 1.0)
    fwd_cos, fwd_sin = tables(detector, -1.0)
    half_real, half_imag = pair_right(frame_real, frame_imag, "qfab,by->qfay", inv_cos, inv_sin)
    field_real, field_imag = pair_right(half_real, half_imag, "qfay,ax->qfyx", perm_cos, perm_sin)
    kernel_real = wigner[0]
    kernel_imag = wigner[1]
    power = kernel_real * kernel_real + kernel_imag * kernel_imag + eps_wiener
    filtered_real = (field_real * kernel_real + field_imag * kernel_imag) / power
    filtered_imag = (field_imag * kernel_real - field_real * kernel_imag) / power
    half_real, half_imag = pair_right(filtered_real, filtered_imag, "qfyx,ax->qfya", fwd_cos, fwd_sin)
    plane_real, plane_imag = pair_right(half_real, half_imag, "qfya,by->qfab", fwd_cos, fwd_sin)
    planes = jnp.stack([plane_real, plane_imag])

    planes = planes.reshape(2, q_block, freq_count, n_det, local_det, detector)
    planes = planes.transpose(3, 0, 1, 2, 4, 5).reshape(n_det, 2 * q_block * freq_count * local_det, detector)
    back = lax.all_to_all(planes, "det", 0, 0, tiled=True)
    back = back.reshape(n_det, 2, q_block, freq_count, local_det, detector).transpose(1, 0, 2, 3, 4, 5)
    return back.reshape(2, n_det * q_block, freq_count, local_det, detector)


def solution(mesh):
    in_specs = (P(None, "scan", None, "det", None), P(None, ("scan", "det"), None, None, None))
    out_specs = P(None, "scan", None, "det", None)
    return jax.shard_map(shards, mesh=mesh, in_specs=in_specs, out_specs=out_specs, check_vma=False)
```

```python
import math

import jax
import jax.numpy as jnp
from jax import lax
from jax.sharding import PartitionSpec as P

eps_wiener = 0.1
MATMUL_PRECISION = lax.Precision.HIGH


def angles(rows, cols, count):
    product = (rows[:, None] * cols[None, :]) % count
    return product.astype(jnp.float32) * (2.0 * math.pi / count)


def tables(count, sign):
    indices = jnp.arange(count, dtype=jnp.int32)
    phases = angles(indices, indices, count)
    norm_scale = 1.0 / math.sqrt(count)
    return (jnp.cos(phases) * norm_scale, sign * jnp.sin(phases) * norm_scale)


def row_table(rows_total, blocks):
    cosine, sines = tables(rows_total, 1.0)
    top = jnp.stack([cosine, sines], axis=1)
    bottom = jnp.stack([-sines, cosine], axis=1)
    full = jnp.stack([top, bottom], axis=1)
    local = rows_total // blocks
    full = full.reshape(rows_total, 2, 2, blocks, local)
    full = full.transpose(0, 1, 3, 2, 4)
    return full.reshape(2 * rows_total, 2 * rows_total)


def product_form(form, left, right):
    return jnp.einsum(form, left, right, precision=MATMUL_PRECISION)


def pair_right(real_in, imag_in, form, cosine, sines):
    real_out = product_form(form, real_in, cosine) - product_form(form, imag_in, sines)
    imag_out = product_form(form, real_in, sines) + product_form(form, imag_in, cosine)
    return (real_out, imag_out)


def one_frequency(data, wigner, n_scan, n_det):
    n_all = n_scan * n_det
    _, local_rows, local_det, detector = data.shape
    rows_total = local_rows * n_scan
    det_total = local_det * n_det
    q_block = rows_total // n_all
    sub = local_det // n_scan

    send = data.reshape(2, local_rows, n_scan, sub, detector).transpose(2, 0, 1, 3, 4)
    send = send.reshape(n_scan, 2 * local_rows, sub * detector)
    got = lax.all_to_all(send, "scan", 0, 0, tiled=True)
    got = got.reshape(2 * rows_total, sub * detector)

    spectra = jnp.dot(row_table(rows_total, n_scan), got, precision=MATMUL_PRECISION)
    spectra = spectra.reshape(n_all, q_block * 2, sub * detector)

    frames = lax.all_to_all(spectra, ("scan", "det"), 0, 0, tiled=True)
    frames = frames.reshape(n_scan, n_det, q_block, 2, sub, detector)
    frames = frames.transpose(2, 3, 0, 1, 4, 5).reshape(q_block, 2, det_total, detector)
    frame_real = frames[:, 0]
    frame_imag = frames[:, 1]

    pos = jnp.arange(det_total, dtype=jnp.int32)
    h_of = pos // (n_det * sub)
    d_of = (pos // sub) % n_det
    a_of = local_det * d_of + sub * h_of + pos % sub
    cols = jnp.arange(detector, dtype=jnp.int32)
    scale = 1.0 / math.sqrt(detector)
    row_phase = angles(a_of, cols, detector)
    perm_cos = jnp.cos(row_phase) * scale
    perm_sin = jnp.sin(row_phase) * scale

    inv_cos, inv_sin = tables(detector, 1.0)
    fwd_cos, fwd_sin = tables(detector, -1.0)
    half_real, half_imag = pair_right(frame_real, frame_imag, "qab,by->qay", inv_cos, inv_sin)
    field_real, field_imag = pair_right(half_real, half_imag, "qay,ax->qyx", perm_cos, perm_sin)
    kernel_real = wigner[0]
    kernel_imag = wigner[1]
    power = kernel_real * kernel_real + kernel_imag * kernel_imag + eps_wiener
    filtered_real = (field_real * kernel_real + field_imag * kernel_imag) / power
    filtered_imag = (field_imag * kernel_real - field_real * kernel_imag) / power
    half_real, half_imag = pair_right(filtered_real, filtered_imag, "qyx,ax->qya", fwd_cos, fwd_sin)
    plane_real, plane_imag = pair_right(half_real, half_imag, "qya,by->qab", fwd_cos, fwd_sin)
    planes = jnp.stack([plane_real, plane_imag])

    planes = planes.reshape(2, q_block, n_det, local_det, detector)
    planes = planes.transpose(2, 0, 1, 3, 4).reshape(n_det, 2 * q_block * local_det, detector)
    back = lax.all_to_all(planes, "det", 0, 0, tiled=True)
    back = back.reshape(n_det, 2, q_block, local_det, detector).transpose(1, 0, 2, 3, 4)
    return back.reshape(2, n_det * q_block, local_det, detector)


def shards(data, wigner):
    n_scan = lax.axis_size("scan")
    n_det = lax.axis_size("det")
    outs = [
        one_frequency(data[:, :, f], wigner[:, :, f], n_scan, n_det) for f in range(data.shape[2])
    ]
    return jnp.stack(outs, axis=2)


def solution(mesh):
    in_specs = (P(None, "scan", None, "det", None), P(None, ("scan", "det"), None, None, None))
    out_specs = P(None, "scan", None, "det", None)
    return jax.shard_map(shards, mesh=mesh, in_specs=in_specs, out_specs=out_specs, check_vma=False)
```

```python
import math

import jax
import jax.numpy as jnp
from jax import lax
from jax.sharding import PartitionSpec as P

eps_wiener = 0.1
MATMUL_PRECISION = lax.Precision.HIGH


def angles(rows, cols, count):
    product = (rows[:, None] * cols[None, :]) % count
    return product.astype(jnp.float32) * (2.0 * math.pi / count)


def tables(count, sign):
    indices = jnp.arange(count, dtype=jnp.int32)
    phases = angles(indices, indices, count)
    norm_scale = 1.0 / math.sqrt(count)
    return (jnp.cos(phases) * norm_scale, sign * jnp.sin(phases) * norm_scale)


def row_table(rows_total, blocks):
    cosine, sines = tables(rows_total, 1.0)
    top = jnp.stack([cosine, sines], axis=1)
    bottom = jnp.stack([-sines, cosine], axis=1)
    full = jnp.stack([top, bottom], axis=1)
    local = rows_total // blocks
    full = full.reshape(rows_total, 2, 2, blocks, local)
    full = full.transpose(0, 1, 3, 2, 4)
    return full.reshape(2 * rows_total, 2 * rows_total)


def product_form(form, left, right):
    return jnp.einsum(form, left, right, precision=MATMUL_PRECISION)


def pair_right(real_in, imag_in, form, cosine, sines):
    real_out = product_form(form, real_in, cosine) - product_form(form, imag_in, sines)
    imag_out = product_form(form, real_in, sines) + product_form(form, imag_in, cosine)
    return (real_out, imag_out)


def shards(data, wigner):
    n_scan = lax.axis_size("scan")
    n_det = lax.axis_size("det")
    n_all = n_scan * n_det
    _, local_rows, freq_count, local_det, detector = data.shape
    rows_total = local_rows * n_scan
    det_total = local_det * n_det
    q_block = rows_total // n_all
    row_parts = max(1, min(local_det // 8, n_scan // freq_count))
    col_parts = n_scan // (freq_count * row_parts)
    row_sub = local_det // row_parts
    col_sub = detector // col_parts

    send = data.reshape(2, local_rows, freq_count, row_parts, row_sub, col_parts, col_sub)
    send = send.transpose(2, 3, 5, 0, 1, 4, 6).reshape(n_scan, 2 * local_rows, row_sub, col_sub)
    got = lax.all_to_all(send, "scan", 0, 0, tiled=True)
    got = got.reshape(2 * rows_total, row_sub, col_sub)

    spectra = jnp.einsum("pk,kmn->pmn", row_table(rows_total, n_scan), got, precision=MATMUL_PRECISION)
    spectra = spectra.reshape(n_all, q_block * 2, row_sub, col_sub)

    frames = lax.all_to_all(spectra, ("scan", "det"), 0, 0, tiled=True)
    frames = frames.reshape(freq_count, row_parts, col_parts, n_det, q_block, 2, row_sub, col_sub)
    frames = frames.transpose(4, 0, 5, 1, 3, 6, 2, 7).reshape(q_block, freq_count, 2, det_total, detector)
    frame_real = frames[:, :, 0]
    frame_imag = frames[:, :, 1]

    pos = jnp.arange(det_total, dtype=jnp.int32)
    h_of = pos // (n_det * row_sub)
    d_of = (pos // row_sub) % n_det
    a_of = local_det * d_of + row_sub * h_of + pos % row_sub
    cols = jnp.arange(detector, dtype=jnp.int32)
    scale = 1.0 / math.sqrt(detector)
    row_phase = angles(a_of, cols, detector)
    perm_cos = jnp.cos(row_phase) * scale
    perm_sin = jnp.sin(row_phase) * scale

    inv_cos, inv_sin = tables(detector, 1.0)
    fwd_cos, fwd_sin = tables(detector, -1.0)
    half_real, half_imag = pair_right(frame_real, frame_imag, "qfab,by->qfay", inv_cos, inv_sin)
    field_real, field_imag = pair_right(half_real, half_imag, "qfay,ax->qfyx", perm_cos, perm_sin)
    kernel_real = wigner[0]
    kernel_imag = wigner[1]
    power = kernel_real * kernel_real + kernel_imag * kernel_imag + eps_wiener
    filtered_real = (field_real * kernel_real + field_imag * kernel_imag) / power
    filtered_imag = (field_imag * kernel_real - field_real * kernel_imag) / power
    half_real, half_imag = pair_right(filtered_real, filtered_imag, "qfyx,ax->qfya", fwd_cos, fwd_sin)
    plane_real, plane_imag = pair_right(half_real, half_imag, "qfya,by->qfab", fwd_cos, fwd_sin)
    planes = jnp.stack([plane_real, plane_imag])

    planes = planes.reshape(2, q_block, freq_count, n_det, local_det, detector)
    planes = planes.transpose(3, 0, 1, 2, 4, 5).reshape(n_det, 2 * q_block * freq_count * local_det, detector)
    back = lax.all_to_all(planes, "det", 0, 0, tiled=True)
    back = back.reshape(n_det, 2, q_block, freq_count, local_det, detector).transpose(1, 0, 2, 3, 4, 5)
    return back.reshape(2, n_det * q_block, freq_count, local_det, detector)


def solution(mesh):
    in_specs = (P(None, "scan", None, "det", None), P(None, ("scan", "det"), None, None, None))
    out_specs = P(None, "scan", None, "det", None)
    return jax.shard_map(shards, mesh=mesh, in_specs=in_specs, out_specs=out_specs, check_vma=False)
```

```python
import math

import jax
import jax.numpy as jnp
from jax import lax
from jax.sharding import PartitionSpec as P

eps_wiener = 0.1
MATMUL_PRECISION = lax.Precision.HIGH


def angles(rows, cols, count):
    product = (rows[:, None] * cols[None, :]) % count
    return product.astype(jnp.float32) * (2.0 * math.pi / count)


def tables(count, sign):
    indices = jnp.arange(count, dtype=jnp.int32)
    phases = angles(indices, indices, count)
    norm_scale = 1.0 / math.sqrt(count)
    return (jnp.cos(phases) * norm_scale, sign * jnp.sin(phases) * norm_scale)


def row_table(rows_total, blocks):
    cosine, sines = tables(rows_total, 1.0)
    top = jnp.stack([cosine, sines], axis=1)
    bottom = jnp.stack([-sines, cosine], axis=1)
    full = jnp.stack([top, bottom], axis=1)
    local = rows_total // blocks
    full = full.reshape(rows_total, 2, 2, blocks, local)
    full = full.transpose(0, 1, 3, 2, 4)
    return full.reshape(2 * rows_total, 2 * rows_total)


def product_form(form, left, right):
    return jnp.einsum(form, left, right, precision=MATMUL_PRECISION)


def pair_right(real_in, imag_in, form, cosine, sines):
    real_out = product_form(form, real_in, cosine) - product_form(form, imag_in, sines)
    imag_out = product_form(form, real_in, sines) + product_form(form, imag_in, cosine)
    return (real_out, imag_out)


def filter_planes(frames, wigner, perm_cos, perm_sin, detector):
    inv_cos, inv_sin = tables(detector, 1.0)
    fwd_cos, fwd_sin = tables(detector, -1.0)
    half_real, half_imag = pair_right(frames[:, :, 0], frames[:, :, 1], "qfab,by->qfay", inv_cos, inv_sin)
    field_real, field_imag = pair_right(half_real, half_imag, "qfay,ax->qfyx", perm_cos, perm_sin)
    kernel_real = wigner[0]
    kernel_imag = wigner[1]
    power = kernel_real * kernel_real + kernel_imag * kernel_imag + eps_wiener
    filtered_real = (field_real * kernel_real + field_imag * kernel_imag) / power
    filtered_imag = (field_imag * kernel_real - field_real * kernel_imag) / power
    half_real, half_imag = pair_right(filtered_real, filtered_imag, "qfyx,ax->qfya", fwd_cos, fwd_sin)
    plane_real, plane_imag = pair_right(half_real, half_imag, "qfya,by->qfab", fwd_cos, fwd_sin)
    return jnp.stack([plane_real, plane_imag])


def shards(data, wigner):
    n_scan = lax.axis_size("scan")
    n_det = lax.axis_size("det")
    n_all = n_scan * n_det
    _, local_rows, freq_count, local_det, detector = data.shape
    rows_total = local_rows * n_scan
    det_total = local_det * n_det
    q_block = rows_total // n_all
    row_parts = max(1, min(local_det // 8, n_scan // freq_count))
    col_parts = n_scan // (freq_count * row_parts)
    row_sub = local_det // row_parts
    col_sub = detector // col_parts

    send = data.reshape(2, local_rows, freq_count, row_parts, row_sub, col_parts, col_sub)
    send = send.transpose(2, 3, 5, 0, 1, 4, 6).reshape(n_scan, 2 * local_rows, row_sub, col_sub)
    got = lax.all_to_all(send, "scan", 0, 0, tiled=True)
    got = got.reshape(2 * rows_total, row_sub, col_sub)

    spectra = jnp.einsum("pk,kmn->pmn", row_table(rows_total, n_scan), got, precision=MATMUL_PRECISION)
    spectra = spectra.reshape(n_all, q_block, 2, row_sub, col_sub)

    pos = jnp.arange(det_total, dtype=jnp.int32)
    h_of = pos // (n_det * row_sub)
    d_of = (pos // row_sub) % n_det
    a_of = local_det * d_of + row_sub * h_of + pos % row_sub
    cols = jnp.arange(detector, dtype=jnp.int32)
    scale = 1.0 / math.sqrt(detector)
    row_phase = angles(a_of, cols, detector)
    perm_cos = jnp.cos(row_phase) * scale
    perm_sin = jnp.sin(row_phase) * scale

    halves = 2 if q_block % 2 == 0 else 1
    part = q_block // halves
    arrived = [
        lax.all_to_all(
            spectra[:, t * part:(t + 1) * part].reshape(n_all, part * 2, row_sub, col_sub),
            ("scan", "det"), 0, 0, tiled=True,
        )
        for t in range(halves)
    ]
    pieces = []
    for t in range(halves):
        frames = arrived[t]
        frames = frames.reshape(freq_count, row_parts, col_parts, n_det, part, 2, row_sub, col_sub)
        frames = frames.transpose(4, 0, 5, 1, 3, 6, 2, 7).reshape(part, freq_count, 2, det_total, detector)
        planes = filter_planes(frames, wigner[:, t * part:(t + 1) * part], perm_cos, perm_sin, detector)
        planes = planes.reshape(2, part, freq_count, n_det, local_det, detector)
        planes = planes.transpose(3, 0, 1, 2, 4, 5).reshape(n_det, 2 * part * freq_count * local_det, detector)
        if t + 1 < halves:
            planes, arrived[t + 1] = lax.optimization_barrier((planes, arrived[t + 1]))
        if pieces:
            planes, pieces[-1] = lax.optimization_barrier((planes, pieces[-1]))
        pieces.append(lax.all_to_all(planes, "det", 0, 0, tiled=True))
    back = jnp.stack(pieces).reshape(halves, n_det, 2, part, freq_count, local_det, detector)
    back = back.transpose(2, 1, 0, 3, 4, 5, 6)
    return back.reshape(2, n_det * q_block, freq_count, local_det, detector)


def solution(mesh):
    in_specs = (P(None, "scan", None, "det", None), P(None, ("scan", "det"), None, None, None))
    out_specs = P(None, "scan", None, "det", None)
    return jax.shard_map(shards, mesh=mesh, in_specs=in_specs, out_specs=out_specs, check_vma=False)
```

```python
import math

import jax
import jax.numpy as jnp
from jax import lax
from jax.sharding import PartitionSpec as P

eps_wiener = 0.1
MATMUL_PRECISION = lax.Precision.HIGH


def angles(rows, cols, count):
    product = (rows[:, None] * cols[None, :]) % count
    return product.astype(jnp.float32) * (2.0 * math.pi / count)


def tables(count, sign):
    indices = jnp.arange(count, dtype=jnp.int32)
    phases = angles(indices, indices, count)
    norm_scale = 1.0 / math.sqrt(count)
    return (jnp.cos(phases) * norm_scale, sign * jnp.sin(phases) * norm_scale)


def row_table(rows_total, blocks):
    cosine, sines = tables(rows_total, 1.0)
    top = jnp.stack([cosine, sines], axis=1)
    bottom = jnp.stack([-sines, cosine], axis=1)
    full = jnp.stack([top, bottom], axis=1)
    local = rows_total // blocks
    full = full.reshape(rows_total, 2, 2, blocks, local)
    full = full.transpose(0, 1, 3, 2, 4)
    return full.reshape(2 * rows_total, 2 * rows_total)


def product_form(form, left, right):
    return jnp.einsum(form, left, right, precision=MATMUL_PRECISION)


def pair_right(real_in, imag_in, form, cosine, sines):
    real_out = product_form(form, real_in, cosine) - product_form(form, imag_in, sines)
    imag_out = product_form(form, real_in, sines) + product_form(form, imag_in, cosine)
    return (real_out, imag_out)


def complex_table(cosine, sines):
    return jnp.block([[cosine, sines], [-sines, cosine]])


def shards(data, wigner):
    n_scan = lax.axis_size("scan")
    n_det = lax.axis_size("det")
    n_all = n_scan * n_det
    _, local_rows, freq_count, local_det, detector = data.shape
    rows_total = local_rows * n_scan
    det_total = local_det * n_det
    q_block = rows_total // n_all
    frame_count = q_block * freq_count
    row_parts = max(1, min(local_det // 8, n_scan // freq_count))
    col_parts = n_scan // (freq_count * row_parts)
    row_sub = local_det // row_parts
    col_sub = detector // col_parts

    send = data.reshape(2, local_rows, freq_count, row_parts, row_sub, col_parts, col_sub)
    send = send.transpose(2, 3, 5, 0, 1, 4, 6).reshape(n_scan, 2 * local_rows, row_sub, col_sub)
    got = lax.all_to_all(send, "scan", 0, 0, tiled=True)
    got = got.reshape(2 * rows_total, row_sub, col_sub)

    spectra = jnp.einsum("pk,kmn->pmn", row_table(rows_total, n_scan), got, precision=MATMUL_PRECISION)
    spectra = spectra.reshape(n_all, q_block * 2, row_sub, col_sub)

    frames = lax.all_to_all(spectra, ("scan", "det"), 0, 0, tiled=True)
    frames = frames.reshape(freq_count, row_parts, col_parts, n_det, q_block, 2, row_sub, col_sub)
    frames = frames.transpose(4, 0, 1, 3, 6, 5, 2, 7).reshape(frame_count * det_total, 2 * detector)

    pos = jnp.arange(det_total, dtype=jnp.int32)
    h_of = pos // (n_det * row_sub)
    d_of = (pos // row_sub) % n_det
    a_of = local_det * d_of + row_sub * h_of + pos % row_sub
    cols = jnp.arange(detector, dtype=jnp.int32)
    scale = 1.0 / math.sqrt(detector)
    row_phase = angles(a_of, cols, detector)
    inv_cos, inv_sin = tables(detector, 1.0)
    fwd_cos, fwd_sin = tables(detector, -1.0)

    half = jnp.dot(frames, complex_table(inv_cos, inv_sin), precision=MATMUL_PRECISION)
    half = half.reshape(frame_count, det_total, 2, detector).transpose(0, 3, 2, 1)
    half = half.reshape(frame_count * detector, 2 * det_total)
    perm_table = complex_table(jnp.cos(row_phase) * scale, jnp.sin(row_phase) * scale)
    field = jnp.dot(half, perm_table, precision=MATMUL_PRECISION)
    field_real = field[:, :detector]
    field_imag = field[:, detector:]
    kernel_real = wigner[0].reshape(frame_count * detector, detector)
    kernel_imag = wigner[1].reshape(frame_count * detector, detector)
    power = kernel_real * kernel_real + kernel_imag * kernel_imag + eps_wiener
    filtered_real = (field_real * kernel_real + field_imag * kernel_imag) / power
    filtered_imag = (field_imag * kernel_real - field_real * kernel_imag) / power
    filtered = jnp.concatenate([filtered_real, filtered_imag], axis=1)

    fwd_table = complex_table(fwd_cos, fwd_sin)
    half = jnp.dot(filtered, fwd_table, precision=MATMUL_PRECISION)
    half = half.reshape(frame_count, detector, 2, det_total).transpose(0, 3, 2, 1)
    half = half.reshape(frame_count * det_total, 2 * detector)
    planes = jnp.dot(half, fwd_table, precision=MATMUL_PRECISION)

    planes = planes.reshape(q_block, freq_count, n_det, local_det, 2, detector)
    planes = planes.transpose(2, 4, 0, 1, 3, 5).reshape(n_det, 2 * q_block * freq_count * local_det, detector)
    back = lax.all_to_all(planes, "det", 0, 0, tiled=True)
    back = back.reshape(n_det, 2, q_block, freq_count, local_det, detector).transpose(1, 0, 2, 3, 4, 5)
    return back.reshape(2, n_det * q_block, freq_count, local_det, detector)


def solution(mesh):
    in_specs = (P(None, "scan", None, "det", None), P(None, ("scan", "det"), None, None, None))
    out_specs = P(None, "scan", None, "det", None)
    return jax.shard_map(shards, mesh=mesh, in_specs=in_specs, out_specs=out_specs, check_vma=False)
```

```python
import math

import jax
import jax.numpy as jnp
from jax import lax
from jax.sharding import PartitionSpec as P

eps_wiener = 0.1
MATMUL_PRECISION = lax.Precision.HIGH


def angles(rows, cols, count):
    product = (rows[:, None] * cols[None, :]) % count
    return product.astype(jnp.float32) * (2.0 * math.pi / count)


def tables(count, sign):
    indices = jnp.arange(count, dtype=jnp.int32)
    phases = angles(indices, indices, count)
    norm_scale = 1.0 / math.sqrt(count)
    return (jnp.cos(phases) * norm_scale, sign * jnp.sin(phases) * norm_scale)


def row_table(rows_total, blocks):
    cosine, sines = tables(rows_total, 1.0)
    top = jnp.stack([cosine, sines], axis=1)
    bottom = jnp.stack([-sines, cosine], axis=1)
    full = jnp.stack([top, bottom], axis=1)
    local = rows_total // blocks
    full = full.reshape(rows_total, 2, 2, blocks, local)
    full = full.transpose(0, 1, 3, 2, 4)
    return full.reshape(2 * rows_total, 2 * rows_total)


def product_form(form, left, right):
    return jnp.einsum(form, left, right, precision=MATMUL_PRECISION)


def pair_right(real_in, imag_in, form, cosine, sines):
    real_out = product_form(form, real_in, cosine) - product_form(form, imag_in, sines)
    imag_out = product_form(form, real_in, sines) + product_form(form, imag_in, cosine)
    return (real_out, imag_out)


def complex_table(cosine, sines):
    return jnp.block([[cosine, sines], [-sines, cosine]])


def shards(data, wigner):
    n_scan = lax.axis_size("scan")
    n_det = lax.axis_size("det")
    n_all = n_scan * n_det
    _, local_rows, freq_count, local_det, detector = data.shape
    rows_total = local_rows * n_scan
    det_total = local_det * n_det
    q_block = rows_total // n_all
    frame_count = q_block * freq_count
    row_parts = max(1, min(local_det // 8, n_scan // freq_count))
    col_parts = n_scan // (freq_count * row_parts)
    row_sub = local_det // row_parts
    col_sub = detector // col_parts

    send = data.reshape(2, local_rows, freq_count, row_parts, row_sub, col_parts, col_sub)
    send = send.transpose(2, 3, 5, 0, 1, 4, 6).reshape(n_scan, 2 * local_rows, row_sub, col_sub)
    got = lax.all_to_all(send, "scan", 0, 0, tiled=True)
    got = got.reshape(2 * rows_total, row_sub, col_sub)

    spectra = jnp.einsum("pk,kmn->pmn", row_table(rows_total, n_scan), got, precision=MATMUL_PRECISION)
    spectra = spectra.reshape(n_all, q_block * 2, row_sub, col_sub)

    frames = lax.all_to_all(spectra, ("scan", "det"), 0, 0, tiled=True)
    frames = frames.reshape(freq_count, row_parts, col_parts, n_det, q_block, 2, row_sub, col_sub)
    frames = frames.transpose(4, 0, 1, 3, 6, 5, 2, 7).reshape(frame_count * det_total, 2 * detector)

    pos = jnp.arange(det_total, dtype=jnp.int32)
    h_of = pos // (n_det * row_sub)
    d_of = (pos // row_sub) % n_det
    a_of = local_det * d_of + row_sub * h_of + pos % row_sub
    cols = jnp.arange(detector, dtype=jnp.int32)
    scale = 1.0 / math.sqrt(detector)
    row_phase = angles(a_of, cols, detector)
    inv_cos, inv_sin = tables(detector, 1.0)
    fwd_cos, fwd_sin = tables(detector, -1.0)

    half = jnp.dot(frames, complex_table(inv_cos, inv_sin), precision=MATMUL_PRECISION)
    half = half.reshape(frame_count, det_total, 2, detector).transpose(0, 3, 2, 1)
    half = half.reshape(frame_count * detector, 2 * det_total)
    perm_table = complex_table(jnp.cos(row_phase) * scale, jnp.sin(row_phase) * scale)
    field = jnp.dot(half, perm_table, precision=MATMUL_PRECISION)
    field_real = field[:, :detector]
    field_imag = field[:, detector:]
    kernel_real = wigner[0].reshape(frame_count * detector, detector)
    kernel_imag = wigner[1].reshape(frame_count * detector, detector)
    power = kernel_real * kernel_real + kernel_imag * kernel_imag + eps_wiener
    filtered_real = (field_real * kernel_real + field_imag * kernel_imag) / power
    filtered_imag = (field_imag * kernel_real - field_real * kernel_imag) / power
    filtered = jnp.concatenate([filtered_real, filtered_imag], axis=1)

    fwd_table = complex_table(fwd_cos, fwd_sin)
    half = jnp.dot(filtered, fwd_table, precision=MATMUL_PRECISION)
    half = half.reshape(q_block, freq_count, detector, 2 * det_total)
    plane_real, plane_imag = pair_right(
        half[..., :det_total], half[..., det_total:], "qfya,by->qfab", fwd_cos, fwd_sin
    )
    planes = jnp.stack([plane_real, plane_imag])

    planes = planes.reshape(2, q_block, freq_count, n_det, local_det, detector)
    planes = planes.transpose(3, 0, 1, 2, 4, 5).reshape(n_det, 2 * q_block * freq_count * local_det, detector)
    back = lax.all_to_all(planes, "det", 0, 0, tiled=True)
    back = back.reshape(n_det, 2, q_block, freq_count, local_det, detector).transpose(1, 0, 2, 3, 4, 5)
    return back.reshape(2, n_det * q_block, freq_count, local_det, detector)


def solution(mesh):
    in_specs = (P(None, "scan", None, "det", None), P(None, ("scan", "det"), None, None, None))
    out_specs = P(None, "scan", None, "det", None)
    return jax.shard_map(shards, mesh=mesh, in_specs=in_specs, out_specs=out_specs, check_vma=False)
```

```python
import math

import jax
import jax.numpy as jnp
from jax import lax
from jax.sharding import PartitionSpec as P

eps_wiener = 0.1
MATMUL_PRECISION = lax.Precision.HIGH


def angles(rows, cols, count):
    product = (rows[:, None] * cols[None, :]) % count
    return product.astype(jnp.float32) * (2.0 * math.pi / count)


def tables(count, sign):
    indices = jnp.arange(count, dtype=jnp.int32)
    phases = angles(indices, indices, count)
    norm_scale = 1.0 / math.sqrt(count)
    return (jnp.cos(phases) * norm_scale, sign * jnp.sin(phases) * norm_scale)


def row_table(rows_total, blocks):
    local = rows_total // blocks
    out_index = lax.broadcasted_iota(jnp.int32, (2 * rows_total, 2 * rows_total), 0)
    in_index = lax.broadcasted_iota(jnp.int32, (2 * rows_total, 2 * rows_total), 1)
    q = out_index // 2
    c_out = out_index % 2
    c_in = (in_index // local) % 2
    r = (in_index // (2 * local)) * local + in_index % local
    phases = ((q * r) % rows_total).astype(jnp.float32) * (2.0 * math.pi / rows_total)
    norm_scale = 1.0 / math.sqrt(rows_total)
    cosine = jnp.cos(phases) * norm_scale
    sines = jnp.sin(phases) * norm_scale
    return jnp.where(c_out == c_in, cosine, jnp.where(c_out == 0, sines, -sines))


def product_form(form, left, right):
    return jnp.einsum(form, left, right, precision=MATMUL_PRECISION)


def pair_right(real_in, imag_in, form, cosine, sines):
    real_out = product_form(form, real_in, cosine) - product_form(form, imag_in, sines)
    imag_out = product_form(form, real_in, sines) + product_form(form, imag_in, cosine)
    return (real_out, imag_out)


def complex_table(cosine, sines):
    return jnp.block([[cosine, sines], [-sines, cosine]])


def shards(data, wigner):
    n_scan = lax.axis_size("scan")
    n_det = lax.axis_size("det")
    n_all = n_scan * n_det
    _, local_rows, freq_count, local_det, detector = data.shape
    rows_total = local_rows * n_scan
    det_total = local_det * n_det
    q_block = rows_total // n_all
    frame_count = q_block * freq_count
    row_parts = max(1, min(local_det // 8, n_scan // freq_count))
    col_parts = n_scan // (freq_count * row_parts)
    row_sub = local_det // row_parts
    col_sub = detector // col_parts

    send = data.reshape(2, local_rows, freq_count, row_parts, row_sub, col_parts, col_sub)
    send = send.transpose(2, 3, 5, 0, 1, 4, 6).reshape(n_scan, 2 * local_rows, row_sub, col_sub)
    got = lax.all_to_all(send, "scan", 0, 0, tiled=True)
    got = got.reshape(2 * rows_total, row_sub, col_sub)

    spectra = jnp.einsum("pk,kmn->pmn", row_table(rows_total, n_scan), got, precision=MATMUL_PRECISION)
    spectra = spectra.reshape(n_all, q_block * 2, row_sub, col_sub)

    frames = lax.all_to_all(spectra, ("scan", "det"), 0, 0, tiled=True)
    frames = frames.reshape(freq_count, row_parts, col_parts, n_det, q_block, 2, row_sub, col_sub)
    frames = frames.transpose(4, 0, 1, 3, 6, 5, 2, 7).reshape(frame_count * det_total, 2 * detector)

    pos = jnp.arange(det_total, dtype=jnp.int32)
    h_of = pos // (n_det * row_sub)
    d_of = (pos // row_sub) % n_det
    a_of = local_det * d_of + row_sub * h_of + pos % row_sub
    cols = jnp.arange(detector, dtype=jnp.int32)
    scale = 1.0 / math.sqrt(detector)
    row_phase = angles(a_of, cols, detector)
    inv_cos, inv_sin = tables(detector, 1.0)
    fwd_cos, fwd_sin = tables(detector, -1.0)

    half = jnp.dot(frames, complex_table(inv_cos, inv_sin), precision=MATMUL_PRECISION)
    half = half.reshape(frame_count, det_total, 2, detector).transpose(0, 3, 2, 1)
    half = half.reshape(frame_count * detector, 2 * det_total)
    perm_table = complex_table(jnp.cos(row_phase) * scale, jnp.sin(row_phase) * scale)
    field = jnp.dot(half, perm_table, precision=MATMUL_PRECISION)
    field_real = field[:, :detector]
    field_imag = field[:, detector:]
    kernel_real = wigner[0].reshape(frame_count * detector, detector)
    kernel_imag = wigner[1].reshape(frame_count * detector, detector)
    power = kernel_real * kernel_real + kernel_imag * kernel_imag + eps_wiener
    gain_real = kernel_real / power
    gain_imag = kernel_imag / power
    filtered_real = field_real * gain_real + field_imag * gain_imag
    filtered_imag = field_imag * gain_real - field_real * gain_imag
    filtered = jnp.concatenate([filtered_real, filtered_imag], axis=1)

    fwd_table = complex_table(fwd_cos, fwd_sin)
    half = jnp.dot(filtered, fwd_table, precision=MATMUL_PRECISION)
    half = half.reshape(q_block, freq_count, detector, 2 * det_total)
    plane_real, plane_imag = pair_right(
        half[..., :det_total], half[..., det_total:], "qfya,by->qfab", fwd_cos, fwd_sin
    )
    planes = jnp.stack([plane_real, plane_imag])

    planes = planes.reshape(2, q_block, freq_count, n_det, local_det, detector)
    planes = planes.transpose(3, 0, 1, 2, 4, 5).reshape(n_det, 2 * q_block * freq_count * local_det, detector)
    back = lax.all_to_all(planes, "det", 0, 0, tiled=True)
    back = back.reshape(n_det, 2, q_block, freq_count, local_det, detector).transpose(1, 0, 2, 3, 4, 5)
    return back.reshape(2, n_det * q_block, freq_count, local_det, detector)


def solution(mesh):
    in_specs = (P(None, "scan", None, "det", None), P(None, ("scan", "det"), None, None, None))
    out_specs = P(None, "scan", None, "det", None)
    return jax.shard_map(shards, mesh=mesh, in_specs=in_specs, out_specs=out_specs, check_vma=False)
```

```python
import math

import jax
import jax.numpy as jnp
from jax import lax
from jax.sharding import PartitionSpec as P

eps_wiener = 0.1
MATMUL_PRECISION = lax.Precision.HIGH


def angles(rows, cols, count):
    product = (rows[:, None] * cols[None, :]) % count
    return product.astype(jnp.float32) * (2.0 * math.pi / count)


def tables(count, sign):
    indices = jnp.arange(count, dtype=jnp.int32)
    phases = angles(indices, indices, count)
    norm_scale = 1.0 / math.sqrt(count)
    return (jnp.cos(phases) * norm_scale, sign * jnp.sin(phases) * norm_scale)


def row_table(rows_total, blocks):
    local = rows_total // blocks
    out_index = lax.broadcasted_iota(jnp.int32, (2 * rows_total, 2 * rows_total), 0)
    in_index = lax.broadcasted_iota(jnp.int32, (2 * rows_total, 2 * rows_total), 1)
    q = out_index // 2
    c_out = out_index % 2
    c_in = (in_index // local) % 2
    r = (in_index // (2 * local)) * local + in_index % local
    phases = ((q * r) % rows_total).astype(jnp.float32) * (2.0 * math.pi / rows_total)
    norm_scale = 1.0 / math.sqrt(rows_total)
    cosine = jnp.cos(phases) * norm_scale
    sines = jnp.sin(phases) * norm_scale
    return jnp.where(c_out == c_in, cosine, jnp.where(c_out == 0, sines, -sines))


def product_form(form, left, right):
    return jnp.einsum(form, left, right, precision=MATMUL_PRECISION)


def pair_right(real_in, imag_in, form, cosine, sines):
    real_out = product_form(form, real_in, cosine) - product_form(form, imag_in, sines)
    imag_out = product_form(form, real_in, sines) + product_form(form, imag_in, cosine)
    return (real_out, imag_out)


def complex_table(cosine, sines):
    return jnp.block([[cosine, sines], [-sines, cosine]])


def shards(data, wigner):
    n_scan = lax.axis_size("scan")
    n_det = lax.axis_size("det")
    n_all = n_scan * n_det
    _, local_rows, freq_count, local_det, detector = data.shape
    rows_total = local_rows * n_scan
    det_total = local_det * n_det
    q_block = rows_total // n_all
    frame_count = q_block * freq_count
    row_parts = max(1, min(local_det // 8, n_scan // freq_count))
    col_parts = n_scan // (freq_count * row_parts)
    row_sub = local_det // row_parts
    col_sub = detector // col_parts

    send = data.reshape(2, local_rows, freq_count, row_parts, row_sub, col_parts, col_sub)
    send = send.transpose(2, 3, 5, 0, 1, 4, 6).reshape(n_scan, 2 * local_rows, row_sub, col_sub)
    table, send = lax.optimization_barrier((row_table(rows_total, n_scan), send))
    got = lax.all_to_all(send, "scan", 0, 0, tiled=True)
    got = got.reshape(2 * rows_total, row_sub, col_sub)

    spectra = jnp.einsum("pk,kmn->pmn", table, got, precision=MATMUL_PRECISION)
    spectra = spectra.reshape(n_all, q_block * 2, row_sub, col_sub)

    frames = lax.all_to_all(spectra, ("scan", "det"), 0, 0, tiled=True)
    frames = frames.reshape(freq_count, row_parts, col_parts, n_det, q_block, 2, row_sub, col_sub)
    frames = frames.transpose(4, 0, 1, 3, 6, 5, 2, 7).reshape(frame_count * det_total, 2 * detector)

    pos = jnp.arange(det_total, dtype=jnp.int32)
    h_of = pos // (n_det * row_sub)
    d_of = (pos // row_sub) % n_det
    a_of = local_det * d_of + row_sub * h_of + pos % row_sub
    cols = jnp.arange(detector, dtype=jnp.int32)
    scale = 1.0 / math.sqrt(detector)
    row_phase = angles(a_of, cols, detector)
    inv_cos, inv_sin = tables(detector, 1.0)
    fwd_cos, fwd_sin = tables(detector, -1.0)

    half = jnp.dot(frames, complex_table(inv_cos, inv_sin), precision=MATMUL_PRECISION)
    half = half.reshape(frame_count, det_total, 2, detector).transpose(0, 3, 2, 1)
    half = half.reshape(frame_count * detector, 2 * det_total)
    perm_table = complex_table(jnp.cos(row_phase) * scale, jnp.sin(row_phase) * scale)
    field = jnp.dot(half, perm_table, precision=MATMUL_PRECISION)
    field_real = field[:, :detector]
    field_imag = field[:, detector:]
    kernel_real = wigner[0].reshape(frame_count * detector, detector)
    kernel_imag = wigner[1].reshape(frame_count * detector, detector)
    power = kernel_real * kernel_real + kernel_imag * kernel_imag + eps_wiener
    filtered_real = (field_real * kernel_real + field_imag * kernel_imag) / power
    filtered_imag = (field_imag * kernel_real - field_real * kernel_imag) / power
    filtered = jnp.concatenate([filtered_real, filtered_imag], axis=1)

    fwd_table = complex_table(fwd_cos, fwd_sin)
    half = jnp.dot(filtered, fwd_table, precision=MATMUL_PRECISION)
    half = half.reshape(q_block, freq_count, detector, 2 * det_total)
    plane_real, plane_imag = pair_right(
        half[..., :det_total], half[..., det_total:], "qfya,by->qfab", fwd_cos, fwd_sin
    )
    planes = jnp.stack([plane_real, plane_imag])

    planes = planes.reshape(2, q_block, freq_count, n_det, local_det, detector)
    planes = planes.transpose(3, 0, 1, 2, 4, 5).reshape(n_det, 2 * q_block * freq_count * local_det, detector)
    back = lax.all_to_all(planes, "det", 0, 0, tiled=True)
    back = back.reshape(n_det, 2, q_block, freq_count, local_det, detector).transpose(1, 0, 2, 3, 4, 5)
    return back.reshape(2, n_det * q_block, freq_count, local_det, detector)


def solution(mesh):
    in_specs = (P(None, "scan", None, "det", None), P(None, ("scan", "det"), None, None, None))
    out_specs = P(None, "scan", None, "det", None)
    return jax.shard_map(shards, mesh=mesh, in_specs=in_specs, out_specs=out_specs, check_vma=False)
```

```python
import math

import jax
import jax.numpy as jnp
from jax import lax
from jax.sharding import PartitionSpec as P

eps_wiener = 0.1
MATMUL_PRECISION = lax.Precision.HIGH


def angles(rows, cols, count):
    product = (rows[:, None] * cols[None, :]) % count
    return product.astype(jnp.float32) * (2.0 * math.pi / count)


def tables(count, sign):
    indices = jnp.arange(count, dtype=jnp.int32)
    phases = angles(indices, indices, count)
    norm_scale = 1.0 / math.sqrt(count)
    return (jnp.cos(phases) * norm_scale, sign * jnp.sin(phases) * norm_scale)


def row_table(rows_total, blocks):
    local = rows_total // blocks
    q = jnp.arange(rows_total, dtype=jnp.int32)
    fine = angles(q, jnp.arange(local, dtype=jnp.int32), rows_total)
    coarse = angles(q, jnp.arange(blocks, dtype=jnp.int32) * local, rows_total)
    norm_scale = 1.0 / math.sqrt(rows_total)
    fine_cos = (jnp.cos(fine) * norm_scale)[:, None, :]
    fine_sin = (jnp.sin(fine) * norm_scale)[:, None, :]
    coarse_cos = jnp.cos(coarse)[:, :, None]
    coarse_sin = jnp.sin(coarse)[:, :, None]
    cosine = fine_cos * coarse_cos - fine_sin * coarse_sin
    sines = fine_sin * coarse_cos + fine_cos * coarse_sin
    top = jnp.stack([cosine, sines], axis=2)
    bottom = jnp.stack([-sines, cosine], axis=2)
    return jnp.stack([top, bottom], axis=1).reshape(2 * rows_total, 2 * rows_total)


def product_form(form, left, right):
    return jnp.einsum(form, left, right, precision=MATMUL_PRECISION)


def pair_right(real_in, imag_in, form, cosine, sines):
    real_out = product_form(form, real_in, cosine) - product_form(form, imag_in, sines)
    imag_out = product_form(form, real_in, sines) + product_form(form, imag_in, cosine)
    return (real_out, imag_out)


def complex_table(cosine, sines):
    return jnp.block([[cosine, sines], [-sines, cosine]])


def shards(data, wigner):
    n_scan = lax.axis_size("scan")
    n_det = lax.axis_size("det")
    n_all = n_scan * n_det
    _, local_rows, freq_count, local_det, detector = data.shape
    rows_total = local_rows * n_scan
    det_total = local_det * n_det
    q_block = rows_total // n_all
    frame_count = q_block * freq_count
    row_parts = max(1, min(local_det // 8, n_scan // freq_count))
    col_parts = n_scan // (freq_count * row_parts)
    row_sub = local_det // row_parts
    col_sub = detector // col_parts

    send = data.reshape(2, local_rows, freq_count, row_parts, row_sub, col_parts, col_sub)
    send = send.transpose(2, 3, 5, 0, 1, 4, 6).reshape(n_scan, 2 * local_rows, row_sub, col_sub)
    table, send = lax.optimization_barrier((row_table(rows_total, n_scan), send))
    got = lax.all_to_all(send, "scan", 0, 0, tiled=True)
    got = got.reshape(2 * rows_total, row_sub, col_sub)

    spectra = jnp.einsum("pk,kmn->pmn", table, got, precision=MATMUL_PRECISION)
    spectra = spectra.reshape(n_all, q_block * 2, row_sub, col_sub)

    frames = lax.all_to_all(spectra, ("scan", "det"), 0, 0, tiled=True)
    frames = frames.reshape(freq_count, row_parts, col_parts, n_det, q_block, 2, row_sub, col_sub)
    frames = frames.transpose(4, 0, 1, 3, 6, 5, 2, 7).reshape(frame_count * det_total, 2 * detector)

    pos = jnp.arange(det_total, dtype=jnp.int32)
    h_of = pos // (n_det * row_sub)
    d_of = (pos // row_sub) % n_det
    a_of = local_det * d_of + row_sub * h_of + pos % row_sub
    cols = jnp.arange(detector, dtype=jnp.int32)
    scale = 1.0 / math.sqrt(detector)
    row_phase = angles(a_of, cols, detector)
    inv_cos, inv_sin = tables(detector, 1.0)
    fwd_cos, fwd_sin = tables(detector, -1.0)

    half = jnp.dot(frames, complex_table(inv_cos, inv_sin), precision=MATMUL_PRECISION)
    half = half.reshape(frame_count, det_total, 2, detector).transpose(0, 3, 2, 1)
    half = half.reshape(frame_count * detector, 2 * det_total)
    perm_table = complex_table(jnp.cos(row_phase) * scale, jnp.sin(row_phase) * scale)
    field = jnp.dot(half, perm_table, precision=MATMUL_PRECISION)
    field_real = field[:, :detector]
    field_imag = field[:, detector:]
    kernel_real = wigner[0].reshape(frame_count * detector, detector)
    kernel_imag = wigner[1].reshape(frame_count * detector, detector)
    power = kernel_real * kernel_real + kernel_imag * kernel_imag + eps_wiener
    filtered_real = (field_real * kernel_real + field_imag * kernel_imag) / power
    filtered_imag = (field_imag * kernel_real - field_real * kernel_imag) / power
    filtered = jnp.concatenate([filtered_real, filtered_imag], axis=1)

    fwd_table = complex_table(fwd_cos, fwd_sin)
    half = jnp.dot(filtered, fwd_table, precision=MATMUL_PRECISION)
    half = half.reshape(q_block, freq_count, detector, 2 * det_total)
    plane_real, plane_imag = pair_right(
        half[..., :det_total], half[..., det_total:], "qfya,by->qfab", fwd_cos, fwd_sin
    )
    planes = jnp.stack([plane_real, plane_imag])

    planes = planes.reshape(2, q_block, freq_count, n_det, local_det, detector)
    planes = planes.transpose(3, 0, 1, 2, 4, 5).reshape(n_det, 2 * q_block * freq_count * local_det, detector)
    back = lax.all_to_all(planes, "det", 0, 0, tiled=True)
    back = back.reshape(n_det, 2, q_block, freq_count, local_det, detector).transpose(1, 0, 2, 3, 4, 5)
    return back.reshape(2, n_det * q_block, freq_count, local_det, detector)


def solution(mesh):
    in_specs = (P(None, "scan", None, "det", None), P(None, ("scan", "det"), None, None, None))
    out_specs = P(None, "scan", None, "det", None)
    return jax.shard_map(shards, mesh=mesh, in_specs=in_specs, out_specs=out_specs, check_vma=False)
```

```python
import math

import jax
import numpy as np
import jax.numpy as jnp
from jax import lax
from jax.sharding import PartitionSpec as P

eps_wiener = 0.1
MATMUL_PRECISION = lax.Precision.HIGH


def angles(rows, cols, count):
    product = (rows[:, None] * cols[None, :]) % count
    return product.astype(jnp.float32) * (2.0 * math.pi / count)


def tables(count, sign):
    indices = jnp.arange(count, dtype=jnp.int32)
    phases = angles(indices, indices, count)
    norm_scale = 1.0 / math.sqrt(count)
    return (jnp.cos(phases) * norm_scale, sign * jnp.sin(phases) * norm_scale)


def row_table(rows_total, blocks):
    local = rows_total // blocks
    q = np.arange(rows_total)[:, None]
    r = np.arange(rows_total)[None, :]
    phases = ((q * r) % rows_total) * (2.0 * np.pi / rows_total)
    cosine = np.cos(phases) / np.sqrt(rows_total)
    sines = np.sin(phases) / np.sqrt(rows_total)
    full = np.stack([np.stack([cosine, sines], axis=1), np.stack([-sines, cosine], axis=1)], axis=1)
    full = full.reshape(rows_total, 2, 2, blocks, local).transpose(0, 1, 3, 2, 4)
    return jnp.asarray(full.reshape(2 * rows_total, 2 * rows_total).astype(np.float32))


def product_form(form, left, right):
    return jnp.einsum(form, left, right, precision=MATMUL_PRECISION)


def pair_right(real_in, imag_in, form, cosine, sines):
    real_out = product_form(form, real_in, cosine) - product_form(form, imag_in, sines)
    imag_out = product_form(form, real_in, sines) + product_form(form, imag_in, cosine)
    return (real_out, imag_out)


def complex_table(cosine, sines):
    return jnp.block([[cosine, sines], [-sines, cosine]])


def shards(data, wigner):
    n_scan = lax.axis_size("scan")
    n_det = lax.axis_size("det")
    n_all = n_scan * n_det
    _, local_rows, freq_count, local_det, detector = data.shape
    rows_total = local_rows * n_scan
    det_total = local_det * n_det
    q_block = rows_total // n_all
    frame_count = q_block * freq_count
    row_parts = max(1, min(local_det // 8, n_scan // freq_count))
    col_parts = n_scan // (freq_count * row_parts)
    row_sub = local_det // row_parts
    col_sub = detector // col_parts

    send = data.reshape(2, local_rows, freq_count, row_parts, row_sub, col_parts, col_sub)
    send = send.transpose(2, 3, 5, 0, 1, 4, 6).reshape(n_scan, 2 * local_rows, row_sub, col_sub)
    got = lax.all_to_all(send, "scan", 0, 0, tiled=True)
    got = got.reshape(2 * rows_total, row_sub, col_sub)

    spectra = jnp.einsum("pk,kmn->pmn", row_table(rows_total, n_scan), got, precision=MATMUL_PRECISION)
    spectra = spectra.reshape(n_all, q_block * 2, row_sub, col_sub)

    frames = lax.all_to_all(spectra, ("scan", "det"), 0, 0, tiled=True)
    frames = frames.reshape(freq_count, row_parts, col_parts, n_det, q_block, 2, row_sub, col_sub)
    frames = frames.transpose(4, 0, 1, 3, 6, 5, 2, 7).reshape(frame_count * det_total, 2 * detector)

    pos = jnp.arange(det_total, dtype=jnp.int32)
    h_of = pos // (n_det * row_sub)
    d_of = (pos // row_sub) % n_det
    a_of = local_det * d_of + row_sub * h_of + pos % row_sub
    cols = jnp.arange(detector, dtype=jnp.int32)
    scale = 1.0 / math.sqrt(detector)
    row_phase = angles(a_of, cols, detector)
    inv_cos, inv_sin = tables(detector, 1.0)
    fwd_cos, fwd_sin = tables(detector, -1.0)

    half = jnp.dot(frames, complex_table(inv_cos, inv_sin), precision=MATMUL_PRECISION)
    half = half.reshape(frame_count, det_total, 2, detector).transpose(0, 3, 2, 1)
    half = half.reshape(frame_count * detector, 2 * det_total)
    perm_table = complex_table(jnp.cos(row_phase) * scale, jnp.sin(row_phase) * scale)
    field = jnp.dot(half, perm_table, precision=MATMUL_PRECISION)
    field_real = field[:, :detector]
    field_imag = field[:, detector:]
    kernel_real = wigner[0].reshape(frame_count * detector, detector)
    kernel_imag = wigner[1].reshape(frame_count * detector, detector)
    power = kernel_real * kernel_real + kernel_imag * kernel_imag + eps_wiener
    filtered_real = (field_real * kernel_real + field_imag * kernel_imag) / power
    filtered_imag = (field_imag * kernel_real - field_real * kernel_imag) / power
    filtered = jnp.concatenate([filtered_real, filtered_imag], axis=1)

    fwd_table = complex_table(fwd_cos, fwd_sin)
    half = jnp.dot(filtered, fwd_table, precision=MATMUL_PRECISION)
    half = half.reshape(q_block, freq_count, detector, 2 * det_total)
    plane_real, plane_imag = pair_right(
        half[..., :det_total], half[..., det_total:], "qfya,by->qfab", fwd_cos, fwd_sin
    )
    planes = jnp.stack([plane_real, plane_imag])

    planes = planes.reshape(2, q_block, freq_count, n_det, local_det, detector)
    planes = planes.transpose(3, 0, 1, 2, 4, 5).reshape(n_det, 2 * q_block * freq_count * local_det, detector)
    back = lax.all_to_all(planes, "det", 0, 0, tiled=True)
    back = back.reshape(n_det, 2, q_block, freq_count, local_det, detector).transpose(1, 0, 2, 3, 4, 5)
    return back.reshape(2, n_det * q_block, freq_count, local_det, detector)


def solution(mesh):
    in_specs = (P(None, "scan", None, "det", None), P(None, ("scan", "det"), None, None, None))
    out_specs = P(None, "scan", None, "det", None)
    return jax.shard_map(shards, mesh=mesh, in_specs=in_specs, out_specs=out_specs, check_vma=False)
```

```python
import math

import jax
import numpy as np
import jax.numpy as jnp
from jax import lax
from jax.sharding import PartitionSpec as P

eps_wiener = 0.1
MATMUL_PRECISION = lax.Precision.HIGH


def angles(rows, cols, count):
    product = (rows[:, None] * cols[None, :]) % count
    return product * (2.0 * np.pi / count)


def tables(count, sign):
    indices = np.arange(count)
    phases = angles(indices, indices, count)
    norm_scale = 1.0 / np.sqrt(count)
    return (np.cos(phases) * norm_scale, sign * np.sin(phases) * norm_scale)


def row_table(rows_total, blocks):
    local = rows_total // blocks
    q = np.arange(rows_total)[:, None]
    r = np.arange(rows_total)[None, :]
    phases = ((q * r) % rows_total) * (2.0 * np.pi / rows_total)
    cosine = np.cos(phases) / np.sqrt(rows_total)
    sines = np.sin(phases) / np.sqrt(rows_total)
    full = np.stack([np.stack([cosine, sines], axis=1), np.stack([-sines, cosine], axis=1)], axis=1)
    full = full.reshape(rows_total, 2, 2, blocks, local).transpose(0, 1, 3, 2, 4)
    return jnp.asarray(full.reshape(2 * rows_total, 2 * rows_total).astype(np.float32))


def product_form(form, left, right):
    return jnp.einsum(form, left, right, precision=MATMUL_PRECISION)


def pair_right(real_in, imag_in, form, cosine, sines):
    real_out = product_form(form, real_in, cosine) - product_form(form, imag_in, sines)
    imag_out = product_form(form, real_in, sines) + product_form(form, imag_in, cosine)
    return (real_out, imag_out)


def complex_table(cosine, sines):
    return jnp.asarray(np.block([[cosine, sines], [-sines, cosine]]).astype(np.float32))


def shards(data, wigner):
    n_scan = lax.axis_size("scan")
    n_det = lax.axis_size("det")
    n_all = n_scan * n_det
    _, local_rows, freq_count, local_det, detector = data.shape
    rows_total = local_rows * n_scan
    det_total = local_det * n_det
    q_block = rows_total // n_all
    frame_count = q_block * freq_count
    row_parts = max(1, min(local_det // 8, n_scan // freq_count))
    col_parts = n_scan // (freq_count * row_parts)
    row_sub = local_det // row_parts
    col_sub = detector // col_parts

    send = data.reshape(2, local_rows, freq_count, row_parts, row_sub, col_parts, col_sub)
    send = send.transpose(2, 3, 5, 0, 1, 4, 6).reshape(n_scan, 2 * local_rows, row_sub, col_sub)
    got = lax.all_to_all(send, "scan", 0, 0, tiled=True)
    got = got.reshape(2 * rows_total, row_sub, col_sub)

    spectra = jnp.einsum("pk,kmn->pmn", row_table(rows_total, n_scan), got, precision=MATMUL_PRECISION)
    spectra = spectra.reshape(n_all, q_block * 2, row_sub, col_sub)

    frames = lax.all_to_all(spectra, ("scan", "det"), 0, 0, tiled=True)
    frames = frames.reshape(freq_count, row_parts, col_parts, n_det, q_block, 2, row_sub, col_sub)
    frames = frames.transpose(4, 0, 1, 3, 6, 5, 2, 7).reshape(frame_count * det_total, 2 * detector)

    pos = np.arange(det_total)
    h_of = pos // (n_det * row_sub)
    d_of = (pos // row_sub) % n_det
    a_of = local_det * d_of + row_sub * h_of + pos % row_sub
    cols = np.arange(detector)
    scale = 1.0 / np.sqrt(detector)
    row_phase = angles(a_of, cols, detector)
    inv_cos, inv_sin = tables(detector, 1.0)
    fwd_cos, fwd_sin = tables(detector, -1.0)

    half = jnp.dot(frames, complex_table(inv_cos, inv_sin), precision=MATMUL_PRECISION)
    half = half.reshape(frame_count, det_total, 2, detector).transpose(0, 3, 2, 1)
    half = half.reshape(frame_count * detector, 2 * det_total)
    perm_table = complex_table(np.cos(row_phase) * scale, np.sin(row_phase) * scale)
    field = jnp.dot(half, perm_table, precision=MATMUL_PRECISION)
    field_real = field[:, :detector]
    field_imag = field[:, detector:]
    kernel_real = wigner[0].reshape(frame_count * detector, detector)
    kernel_imag = wigner[1].reshape(frame_count * detector, detector)
    power = kernel_real * kernel_real + kernel_imag * kernel_imag + eps_wiener
    filtered_real = (field_real * kernel_real + field_imag * kernel_imag) / power
    filtered_imag = (field_imag * kernel_real - field_real * kernel_imag) / power
    filtered = jnp.concatenate([filtered_real, filtered_imag], axis=1)

    fwd_table = complex_table(fwd_cos, fwd_sin)
    half = jnp.dot(filtered, fwd_table, precision=MATMUL_PRECISION)
    half = half.reshape(q_block, freq_count, detector, 2 * det_total)
    plane_real, plane_imag = pair_right(
        half[..., :det_total], half[..., det_total:], "qfya,by->qfab",
        jnp.asarray(fwd_cos.astype(np.float32)), jnp.asarray(fwd_sin.astype(np.float32)),
    )
    planes = jnp.stack([plane_real, plane_imag])

    planes = planes.reshape(2, q_block, freq_count, n_det, local_det, detector)
    planes = planes.transpose(3, 0, 1, 2, 4, 5).reshape(n_det, 2 * q_block * freq_count * local_det, detector)
    back = lax.all_to_all(planes, "det", 0, 0, tiled=True)
    back = back.reshape(n_det, 2, q_block, freq_count, local_det, detector).transpose(1, 0, 2, 3, 4, 5)
    return back.reshape(2, n_det * q_block, freq_count, local_det, detector)


def solution(mesh):
    in_specs = (P(None, "scan", None, "det", None), P(None, ("scan", "det"), None, None, None))
    out_specs = P(None, "scan", None, "det", None)
    return jax.shard_map(shards, mesh=mesh, in_specs=in_specs, out_specs=out_specs, check_vma=False)
```

```python
import math

import jax
import numpy as np
import jax.numpy as jnp
from jax import lax
from jax.sharding import PartitionSpec as P

eps_wiener = 0.1
MATMUL_PRECISION = lax.Precision.HIGH


def angles(rows, cols, count):
    product = (rows[:, None] * cols[None, :]) % count
    return product * (2.0 * np.pi / count)


def tables(count, sign):
    indices = np.arange(count)
    phases = angles(indices, indices, count)
    norm_scale = 1.0 / np.sqrt(count)
    return (np.cos(phases) * norm_scale, sign * np.sin(phases) * norm_scale)


def row_table(rows_total, blocks):
    local = rows_total // blocks
    q = np.arange(rows_total)[:, None]
    r = np.arange(rows_total)[None, :]
    phases = ((q * r) % rows_total) * (2.0 * np.pi / rows_total)
    cosine = np.cos(phases) / np.sqrt(rows_total)
    sines = np.sin(phases) / np.sqrt(rows_total)
    full = np.stack([np.stack([cosine, sines], axis=1), np.stack([-sines, cosine], axis=1)], axis=1)
    full = full.reshape(rows_total, 2, 2, blocks, local).transpose(0, 1, 3, 2, 4)
    return jnp.asarray(full.reshape(2 * rows_total, 2 * rows_total).astype(np.float32))


def product_form(form, left, right):
    return jnp.einsum(form, left, right, precision=MATMUL_PRECISION)


def pair_right(real_in, imag_in, form, cosine, sines):
    real_out = product_form(form, real_in, cosine) - product_form(form, imag_in, sines)
    imag_out = product_form(form, real_in, sines) + product_form(form, imag_in, cosine)
    return (real_out, imag_out)


def complex_table(cosine, sines):
    return jnp.asarray(np.block([[cosine, sines], [-sines, cosine]]).astype(np.float32))


def shards(data, wigner):
    n_scan = lax.axis_size("scan")
    n_det = lax.axis_size("det")
    n_all = n_scan * n_det
    _, local_rows, freq_count, local_det, detector = data.shape
    rows_total = local_rows * n_scan
    det_total = local_det * n_det
    q_block = rows_total // n_all
    frame_count = q_block * freq_count
    row_parts = max(1, min(local_det // 8, n_scan // freq_count))
    col_parts = n_scan // (freq_count * row_parts)
    row_sub = local_det // row_parts
    col_sub = detector // col_parts

    send = data.reshape(2, local_rows, freq_count, row_parts, row_sub, col_parts, col_sub)
    send = send.transpose(2, 3, 5, 0, 1, 4, 6).reshape(n_scan, 2 * local_rows, row_sub, col_sub)
    got = lax.all_to_all(send, "scan", 0, 0, tiled=True)
    got = got.reshape(2 * rows_total, row_sub, col_sub)

    spectra = jnp.einsum("pk,kmn->pmn", row_table(rows_total, n_scan), got, precision=MATMUL_PRECISION)
    spectra = spectra.reshape(n_all, q_block * 2, row_sub, col_sub)

    frames = lax.all_to_all(spectra, ("scan", "det"), 0, 0, tiled=True)
    frames, wigner = lax.optimization_barrier((frames, wigner))
    frames = frames.reshape(freq_count, row_parts, col_parts, n_det, q_block, 2, row_sub, col_sub)
    frames = frames.transpose(4, 0, 1, 3, 6, 5, 2, 7).reshape(frame_count * det_total, 2 * detector)

    pos = np.arange(det_total)
    h_of = pos // (n_det * row_sub)
    d_of = (pos // row_sub) % n_det
    a_of = local_det * d_of + row_sub * h_of + pos % row_sub
    cols = np.arange(detector)
    scale = 1.0 / np.sqrt(detector)
    row_phase = angles(a_of, cols, detector)
    inv_cos, inv_sin = tables(detector, 1.0)
    fwd_cos, fwd_sin = tables(detector, -1.0)

    half = jnp.dot(frames, complex_table(inv_cos, inv_sin), precision=MATMUL_PRECISION)
    half = half.reshape(frame_count, det_total, 2, detector).transpose(0, 3, 2, 1)
    half = half.reshape(frame_count * detector, 2 * det_total)
    perm_table = complex_table(np.cos(row_phase) * scale, np.sin(row_phase) * scale)
    field = jnp.dot(half, perm_table, precision=MATMUL_PRECISION)
    field_real = field[:, :detector]
    field_imag = field[:, detector:]
    kernel_real = wigner[0].reshape(frame_count * detector, detector)
    kernel_imag = wigner[1].reshape(frame_count * detector, detector)
    power = kernel_real * kernel_real + kernel_imag * kernel_imag + eps_wiener
    filtered_real = (field_real * kernel_real + field_imag * kernel_imag) / power
    filtered_imag = (field_imag * kernel_real - field_real * kernel_imag) / power
    filtered = jnp.concatenate([filtered_real, filtered_imag], axis=1)

    fwd_table = complex_table(fwd_cos, fwd_sin)
    half = jnp.dot(filtered, fwd_table, precision=MATMUL_PRECISION)
    half = half.reshape(q_block, freq_count, detector, 2 * det_total)
    plane_real, plane_imag = pair_right(
        half[..., :det_total], half[..., det_total:], "qfya,by->qfab",
        jnp.asarray(fwd_cos.astype(np.float32)), jnp.asarray(fwd_sin.astype(np.float32)),
    )
    planes = jnp.stack([plane_real, plane_imag])

    planes = planes.reshape(2, q_block, freq_count, n_det, local_det, detector)
    planes = planes.transpose(3, 0, 1, 2, 4, 5).reshape(n_det, 2 * q_block * freq_count * local_det, detector)
    back = lax.all_to_all(planes, "det", 0, 0, tiled=True)
    back = back.reshape(n_det, 2, q_block, freq_count, local_det, detector).transpose(1, 0, 2, 3, 4, 5)
    return back.reshape(2, n_det * q_block, freq_count, local_det, detector)


def solution(mesh):
    in_specs = (P(None, "scan", None, "det", None), P(None, ("scan", "det"), None, None, None))
    out_specs = P(None, "scan", None, "det", None)
    return jax.shard_map(shards, mesh=mesh, in_specs=in_specs, out_specs=out_specs, check_vma=False)
```

```python
import math

import jax
import numpy as np
import jax.numpy as jnp
from jax import lax
from jax.sharding import PartitionSpec as P

eps_wiener = 0.1
MATMUL_PRECISION = lax.Precision.HIGH


def angles(rows, cols, count):
    product = (rows[:, None] * cols[None, :]) % count
    return product * (2.0 * np.pi / count)


def tables(count, sign):
    indices = np.arange(count)
    phases = angles(indices, indices, count)
    norm_scale = 1.0 / np.sqrt(count)
    return (np.cos(phases) * norm_scale, sign * np.sin(phases) * norm_scale)


def row_table(rows_total, blocks):
    local = rows_total // blocks
    q = np.arange(rows_total)[:, None]
    r = np.arange(rows_total)[None, :]
    phases = ((q * r) % rows_total) * (2.0 * np.pi / rows_total)
    cosine = np.cos(phases) / np.sqrt(rows_total)
    sines = np.sin(phases) / np.sqrt(rows_total)
    full = np.stack([np.stack([cosine, sines], axis=1), np.stack([-sines, cosine], axis=1)], axis=1)
    full = full.reshape(rows_total, 2, 2, blocks, local).transpose(0, 1, 3, 2, 4)
    return jnp.asarray(full.reshape(2 * rows_total, 2 * rows_total).astype(np.float32))


def product_form(form, left, right):
    return jnp.einsum(form, left, right, precision=MATMUL_PRECISION)


def pair_right(real_in, imag_in, form, cosine, sines):
    real_out = product_form(form, real_in, cosine) - product_form(form, imag_in, sines)
    imag_out = product_form(form, real_in, sines) + product_form(form, imag_in, cosine)
    return (real_out, imag_out)


def complex_table(cosine, sines):
    return jnp.asarray(np.block([[cosine, sines], [-sines, cosine]]).astype(np.float32))


def shards(data, wigner):
    n_scan = lax.axis_size("scan")
    n_det = lax.axis_size("det")
    n_all = n_scan * n_det
    _, local_rows, freq_count, local_det, detector = data.shape
    rows_total = local_rows * n_scan
    det_total = local_det * n_det
    q_block = rows_total // n_all
    frame_count = q_block * freq_count
    row_parts = max(1, min(local_det // 8, n_scan // freq_count))
    col_parts = n_scan // (freq_count * row_parts)
    row_sub = local_det // row_parts
    col_sub = detector // col_parts

    send = data.reshape(2, local_rows, freq_count, row_parts, row_sub, col_parts, col_sub)
    send = send.transpose(2, 3, 5, 0, 1, 4, 6).reshape(n_scan, 2 * local_rows, row_sub, col_sub)
    got = lax.all_to_all(send, "scan", 0, 0, tiled=True)
    got = got.reshape(2 * rows_total, row_sub, col_sub)

    spectra = jnp.einsum("pk,kmn->pmn", row_table(rows_total, n_scan), got, precision=MATMUL_PRECISION)
    spectra = spectra.reshape(n_all, q_block * 2, row_sub, col_sub)

    frames = lax.all_to_all(spectra, ("scan", "det"), 0, 0, tiled=True)
    frames, wigner = lax.optimization_barrier((frames, wigner))
    frames = frames.reshape(freq_count, row_parts, col_parts, n_det, q_block, 2, row_sub, col_sub)
    frames = frames.transpose(4, 0, 1, 3, 6, 5, 2, 7).reshape(frame_count * det_total, 2 * detector)

    pos = np.arange(det_total)
    h_of = pos // (n_det * row_sub)
    d_of = (pos // row_sub) % n_det
    a_of = local_det * d_of + row_sub * h_of + pos % row_sub
    cols = np.arange(detector)
    scale = 1.0 / np.sqrt(detector)
    row_phase = angles(a_of, cols, detector)
    inv_cos, inv_sin = tables(detector, 1.0)
    fwd_cos, fwd_sin = tables(detector, -1.0)

    half = jnp.dot(frames, complex_table(inv_cos, inv_sin), precision=MATMUL_PRECISION)
    half = half.reshape(frame_count, det_total * 2, detector)
    perm_cos = np.cos(row_phase) * scale
    perm_sin = np.sin(row_phase) * scale
    perm_table = np.stack([np.concatenate([perm_cos, perm_sin], 1), np.concatenate([-perm_sin, perm_cos], 1)], 1)
    perm_table = jnp.asarray(perm_table.reshape(det_total * 2, 2 * detector).astype(np.float32))
    field = jnp.einsum("zky,kx->zyx", half, perm_table, precision=MATMUL_PRECISION)
    field = field.reshape(frame_count * detector, 2 * detector)
    field_real = field[:, :detector]
    field_imag = field[:, detector:]
    kernel_real = wigner[0].reshape(frame_count * detector, detector)
    kernel_imag = wigner[1].reshape(frame_count * detector, detector)
    power = kernel_real * kernel_real + kernel_imag * kernel_imag + eps_wiener
    filtered_real = (field_real * kernel_real + field_imag * kernel_imag) / power
    filtered_imag = (field_imag * kernel_real - field_real * kernel_imag) / power
    filtered = jnp.concatenate([filtered_real, filtered_imag], axis=1)

    fwd_table = complex_table(fwd_cos, fwd_sin)
    half = jnp.dot(filtered, fwd_table, precision=MATMUL_PRECISION)
    half = half.reshape(q_block, freq_count, detector, 2 * det_total)
    plane_real, plane_imag = pair_right(
        half[..., :det_total], half[..., det_total:], "qfya,by->qfab",
        jnp.asarray(fwd_cos.astype(np.float32)), jnp.asarray(fwd_sin.astype(np.float32)),
    )
    planes = jnp.stack([plane_real, plane_imag])

    planes = planes.reshape(2, q_block, freq_count, n_det, local_det, detector)
    planes = planes.transpose(3, 0, 1, 2, 4, 5).reshape(n_det, 2 * q_block * freq_count * local_det, detector)
    back = lax.all_to_all(planes, "det", 0, 0, tiled=True)
    back = back.reshape(n_det, 2, q_block, freq_count, local_det, detector).transpose(1, 0, 2, 3, 4, 5)
    return back.reshape(2, n_det * q_block, freq_count, local_det, detector)


def solution(mesh):
    in_specs = (P(None, "scan", None, "det", None), P(None, ("scan", "det"), None, None, None))
    out_specs = P(None, "scan", None, "det", None)
    return jax.shard_map(shards, mesh=mesh, in_specs=in_specs, out_specs=out_specs, check_vma=False)
```

```python
import math

import jax
import numpy as np
import jax.numpy as jnp
from jax import lax
from jax.sharding import PartitionSpec as P

eps_wiener = 0.1
MATMUL_PRECISION = lax.Precision.HIGH


def angles(rows, cols, count):
    product = (rows[:, None] * cols[None, :]) % count
    return product * (2.0 * np.pi / count)


def tables(count, sign):
    indices = np.arange(count)
    phases = angles(indices, indices, count)
    norm_scale = 1.0 / np.sqrt(count)
    return (np.cos(phases) * norm_scale, sign * np.sin(phases) * norm_scale)


def row_table(rows_total, blocks):
    local = rows_total // blocks
    q = np.arange(rows_total)[:, None]
    r = np.arange(rows_total)[None, :]
    phases = ((q * r) % rows_total) * (2.0 * np.pi / rows_total)
    cosine = np.cos(phases) / np.sqrt(rows_total)
    sines = np.sin(phases) / np.sqrt(rows_total)
    full = np.stack([np.stack([cosine, sines], axis=1), np.stack([-sines, cosine], axis=1)], axis=1)
    full = full.reshape(rows_total, 2, 2, blocks, local).transpose(0, 1, 3, 2, 4)
    return jnp.asarray(full.reshape(2 * rows_total, 2 * rows_total).astype(np.float32))


def product_form(form, left, right):
    return jnp.einsum(form, left, right, precision=MATMUL_PRECISION)


def pair_right(real_in, imag_in, form, cosine, sines):
    real_out = product_form(form, real_in, cosine) - product_form(form, imag_in, sines)
    imag_out = product_form(form, real_in, sines) + product_form(form, imag_in, cosine)
    return (real_out, imag_out)


def complex_table(cosine, sines):
    return jnp.asarray(np.block([[cosine, sines], [-sines, cosine]]).astype(np.float32))


def shards(data, wigner):
    n_scan = lax.axis_size("scan")
    n_det = lax.axis_size("det")
    n_all = n_scan * n_det
    _, local_rows, freq_count, local_det, detector = data.shape
    rows_total = local_rows * n_scan
    det_total = local_det * n_det
    q_block = rows_total // n_all
    frame_count = q_block * freq_count
    row_parts = max(1, min(local_det // 8, n_scan // freq_count))
    col_parts = n_scan // (freq_count * row_parts)
    row_sub = local_det // row_parts
    col_sub = detector // col_parts

    send = data.reshape(2, local_rows, freq_count, row_parts, row_sub, col_parts, col_sub)
    send = send.transpose(2, 3, 5, 0, 1, 4, 6).reshape(n_scan, 2 * local_rows, row_sub, col_sub)
    got = lax.all_to_all(send, "scan", 0, 0, tiled=True)
    got = got.reshape(2 * rows_total, row_sub, col_sub)

    spectra = jnp.einsum("pk,kmn->pmn", row_table(rows_total, n_scan), got, precision=MATMUL_PRECISION)
    spectra = spectra.reshape(n_all, q_block * 2, row_sub, col_sub)

    frames = lax.all_to_all(spectra, ("scan", "det"), 0, 0, tiled=True)
    frames, wigner = lax.optimization_barrier((frames, wigner))
    frames = frames.reshape(freq_count, row_parts, col_parts, n_det, q_block, 2, row_sub, col_sub)
    frames = frames.transpose(4, 0, 1, 3, 6, 5, 2, 7).reshape(frame_count * det_total, 2 * detector)

    pos = np.arange(det_total)
    h_of = pos // (n_det * row_sub)
    d_of = (pos // row_sub) % n_det
    a_of = local_det * d_of + row_sub * h_of + pos % row_sub
    cols = np.arange(detector)
    scale = 1.0 / np.sqrt(detector)
    row_phase = angles(a_of, cols, detector)
    inv_cos, inv_sin = tables(detector, 1.0)
    fwd_cos, fwd_sin = tables(detector, -1.0)

    half = jnp.dot(frames, complex_table(inv_cos, inv_sin), precision=MATMUL_PRECISION)
    half = half.reshape(frame_count, det_total, 2, detector).transpose(0, 3, 2, 1)
    half = half.reshape(frame_count * detector, 2 * det_total)
    perm_table = complex_table(np.cos(row_phase) * scale, np.sin(row_phase) * scale)
    field = jnp.dot(half, perm_table, precision=MATMUL_PRECISION)
    field_real = field[:, :detector]
    field_imag = field[:, detector:]
    kernel_real = wigner[0].reshape(frame_count * detector, detector)
    kernel_imag = wigner[1].reshape(frame_count * detector, detector)
    power = kernel_real * kernel_real + kernel_imag * kernel_imag + eps_wiener
    filtered_real = (field_real * kernel_real + field_imag * kernel_imag) / power
    filtered_imag = (field_imag * kernel_real - field_real * kernel_imag) / power
    filtered = jnp.concatenate([filtered_real, filtered_imag], axis=1)

    fwd_table = complex_table(fwd_cos, fwd_sin)
    half = jnp.dot(filtered, fwd_table, precision=MATMUL_PRECISION)
    half = half.reshape(q_block, freq_count, detector, 2 * det_total)
    both = jnp.asarray(np.concatenate([fwd_cos, fwd_sin], axis=1).astype(np.float32))
    parts = jnp.einsum("qfyp,yn->qfpn", half, both, precision=MATMUL_PRECISION)
    plane_real = parts[:, :, :det_total, :detector] - parts[:, :, det_total:, detector:]
    plane_imag = parts[:, :, det_total:, :detector] + parts[:, :, :det_total, detector:]
    planes = jnp.stack([plane_real, plane_imag])

    planes = planes.reshape(2, q_block, freq_count, n_det, local_det, detector)
    planes = planes.transpose(3, 0, 1, 2, 4, 5).reshape(n_det, 2 * q_block * freq_count * local_det, detector)
    back = lax.all_to_all(planes, "det", 0, 0, tiled=True)
    back = back.reshape(n_det, 2, q_block, freq_count, local_det, detector).transpose(1, 0, 2, 3, 4, 5)
    return back.reshape(2, n_det * q_block, freq_count, local_det, detector)


def solution(mesh):
    in_specs = (P(None, "scan", None, "det", None), P(None, ("scan", "det"), None, None, None))
    out_specs = P(None, "scan", None, "det", None)
    return jax.shard_map(shards, mesh=mesh, in_specs=in_specs, out_specs=out_specs, check_vma=False)
```

```python
import math

import jax
import numpy as np
import jax.numpy as jnp
from jax import lax
from jax.sharding import PartitionSpec as P

eps_wiener = 0.1
MATMUL_PRECISION = lax.Precision.HIGH


def angles(rows, cols, count):
    product = (rows[:, None] * cols[None, :]) % count
    return product * (2.0 * np.pi / count)


def tables(count, sign):
    indices = np.arange(count)
    phases = angles(indices, indices, count)
    norm_scale = 1.0 / np.sqrt(count)
    return (np.cos(phases) * norm_scale, sign * np.sin(phases) * norm_scale)


def row_table(rows_total, blocks):
    local = rows_total // blocks
    q = np.arange(rows_total)[:, None]
    r = np.arange(rows_total)[None, :]
    phases = ((q * r) % rows_total) * (2.0 * np.pi / rows_total)
    cosine = np.cos(phases) / np.sqrt(rows_total)
    sines = np.sin(phases) / np.sqrt(rows_total)
    full = np.stack([np.stack([cosine, sines], axis=1), np.stack([-sines, cosine], axis=1)], axis=1)
    full = full.reshape(rows_total, 2, 2, blocks, local).transpose(0, 1, 3, 2, 4)
    return jnp.asarray(full.reshape(2 * rows_total, 2 * rows_total).astype(np.float32))


def product_form(form, left, right):
    return jnp.einsum(form, left, right, precision=MATMUL_PRECISION)


def pair_right(real_in, imag_in, form, cosine, sines):
    real_out = product_form(form, real_in, cosine) - product_form(form, imag_in, sines)
    imag_out = product_form(form, real_in, sines) + product_form(form, imag_in, cosine)
    return (real_out, imag_out)


def complex_table(cosine, sines):
    return jnp.asarray(np.block([[cosine, sines], [-sines, cosine]]).astype(np.float32))


def shards(data, wigner):
    n_scan = lax.axis_size("scan")
    n_det = lax.axis_size("det")
    n_all = n_scan * n_det
    _, local_rows, freq_count, local_det, detector = data.shape
    rows_total = local_rows * n_scan
    det_total = local_det * n_det
    q_block = rows_total // n_all
    frame_count = q_block * freq_count
    row_parts = max(1, min(local_det // 8, n_scan // freq_count))
    col_parts = n_scan // (freq_count * row_parts)
    row_sub = local_det // row_parts
    col_sub = detector // col_parts

    send = data.reshape(2, local_rows, freq_count, row_parts, row_sub, col_parts, col_sub)
    send = send.transpose(2, 3, 5, 0, 1, 4, 6).reshape(n_scan, 2 * local_rows, row_sub, col_sub)
    got = lax.all_to_all(send, "scan", 0, 0, tiled=True)
    got = got.reshape(2 * rows_total, row_sub, col_sub)

    spectra = jnp.einsum("pk,kmn->pmn", row_table(rows_total, n_scan), got, precision=MATMUL_PRECISION)
    spectra = spectra.reshape(n_all, q_block * 2, row_sub, col_sub)

    frames = lax.all_to_all(spectra, ("scan", "det"), 0, 0, tiled=True)
    frames, wigner = lax.optimization_barrier((frames, wigner))
    frames = frames.reshape(freq_count, row_parts, col_parts, n_det, q_block, 2, row_sub, col_sub)
    frames = frames.transpose(4, 0, 1, 3, 6, 5, 2, 7).reshape(frame_count * det_total, 2 * detector)

    pos = np.arange(det_total)
    h_of = pos // (n_det * row_sub)
    d_of = (pos // row_sub) % n_det
    a_of = local_det * d_of + row_sub * h_of + pos % row_sub
    cols = np.arange(detector)
    scale = 1.0 / np.sqrt(detector)
    row_phase = angles(a_of, cols, detector)
    inv_cos, inv_sin = tables(detector, 1.0)
    fwd_cos, fwd_sin = tables(detector, -1.0)

    half = jnp.dot(frames, complex_table(inv_cos, inv_sin), precision=MATMUL_PRECISION)
    half = half.reshape(frame_count, det_total, 2 * detector)
    perm_both = np.concatenate([np.cos(row_phase) * scale, np.sin(row_phase) * scale], axis=1)
    parts = jnp.einsum("zap,an->zpn", half, jnp.asarray(perm_both.astype(np.float32)), precision=MATMUL_PRECISION)
    field_real = (parts[:, :detector, :detector] - parts[:, detector:, detector:]).reshape(-1, detector)
    field_imag = (parts[:, :detector, detector:] + parts[:, detector:, :detector]).reshape(-1, detector)
    kernel_real = wigner[0].reshape(frame_count * detector, detector)
    kernel_imag = wigner[1].reshape(frame_count * detector, detector)
    power = kernel_real * kernel_real + kernel_imag * kernel_imag + eps_wiener
    filtered_real = (field_real * kernel_real + field_imag * kernel_imag) / power
    filtered_imag = (field_imag * kernel_real - field_real * kernel_imag) / power
    filtered = jnp.concatenate([filtered_real, filtered_imag], axis=1)

    fwd_table = complex_table(fwd_cos, fwd_sin)
    half = jnp.dot(filtered, fwd_table, precision=MATMUL_PRECISION)
    half = half.reshape(q_block, freq_count, detector, 2 * det_total)
    both = jnp.asarray(np.concatenate([fwd_cos, fwd_sin], axis=1).astype(np.float32))
    parts = jnp.einsum("qfyp,yn->qfpn", half, both, precision=MATMUL_PRECISION)
    plane_real = parts[:, :, :det_total, :detector] - parts[:, :, det_total:, detector:]
    plane_imag = parts[:, :, det_total:, :detector] + parts[:, :, :det_total, detector:]
    planes = jnp.stack([plane_real, plane_imag])

    planes = planes.reshape(2, q_block, freq_count, n_det, local_det, detector)
    planes = planes.transpose(3, 0, 1, 2, 4, 5).reshape(n_det, 2 * q_block * freq_count * local_det, detector)
    back = lax.all_to_all(planes, "det", 0, 0, tiled=True)
    back = back.reshape(n_det, 2, q_block, freq_count, local_det, detector).transpose(1, 0, 2, 3, 4, 5)
    return back.reshape(2, n_det * q_block, freq_count, local_det, detector)


def solution(mesh):
    in_specs = (P(None, "scan", None, "det", None), P(None, ("scan", "det"), None, None, None))
    out_specs = P(None, "scan", None, "det", None)
    return jax.shard_map(shards, mesh=mesh, in_specs=in_specs, out_specs=out_specs, check_vma=False)
```
